256 devices in a mesh: rows: 16 (over z, y_hi), bx: 4 (over y_lo, core), by: 4 (over x).
Axes of the slice: x: 4, y: 4 (y_hi: 2, y_lo: 2; y = y_hi * 2 + y_lo), z: 8, core: 2. Of those that a mesh axis runs over, the one named last changes fastest.
Arguments:
- pair_mult: bfloat16 [1048576, 256], P(('rows', 'bx', 'by')), may hold values from -1.5 to 1.5
- pair_dens: float32 [1048576], P(('rows', 'bx', 'by')), may hold values from -3 to 3
- pair_live: int32 [1048576], P(('rows', 'bx', 'by')), may hold values 0 or 1
- pair_box: int32 [1048576], P(('rows', 'bx', 'by')), may hold values from 0 to 767
- inter_mask: int32 [128, 32, 32, 98], P('rows', 'bx', 'by'), may hold values 0 or 1
- row_scale: float32 [98, 256], replicated, may hold values from 0.3 to 1.5
- col_scale: float32 [98, 256], replicated, may hold values from 0.3 to 1.5
- base: bfloat16 [256, 256], replicated, may hold values from -0.0390625 to 0.0390625
- lattice: float32 [256, 256], replicated, may hold values from -0.0009765625 to 0.0009765625
Outputs:
- box_locals: bfloat16 [128, 32, 32, 256], P('rows', 'bx', 'by')
- pair_j: float32 [1048576], P(('rows', 'bx', 'by'))
The draws below stay inside these ranges and needn't reach their ends.
Inputs may be any that keep to these rules, and one draw needn't show every extreme that they name: `pair_box`: numbers a box of the pair's own x, y slab as (l * 8 + x) * 8 + y with l in 0..11, x in 0..7, y in 0..7, where level l is the box z = (rows index of the device * 8 + l - 2) mod 128.
All inputs are finite; a program needn't handle non-finite values. No bound on the sum of `pair_live` or of `inter_mask` on one device may be relied on, other than what follows from the above.
Results may differ from the reference program's by a relative error of at most 0.007.
Values may be sent and summed in bfloat16 or wider, within the bound.
No kernel may reach another device: no remote copies, remote signals or barrier semaphores. Data moves between devices by JAX's collectives and lax.ppermute only.
A program may use at most 128 MiB of HBM per device.

```python
import math
import jax
import jax.numpy as jnp
import numpy as np
from jax import lax

NC = 256
OFFS = 98
BXL = 8
BYL = 8
BZL = 8
PAIR_DEV = 4096
NBX = 32
NBY = 32
NBZ = 128
NEAR = 768
PAIRS = 1048576
N_BX = 4
N_BY = 4
DEVICES = 256


def place_ends(result, stream_key, smallest, high):
    place = [jax.random.randint(jax.random.fold_in(stream_key, axis), (), 0, length) for axis, length in enumerate(result.shape)]
    widest = result.shape.index(max(result.shape))
    beside = place[:widest] + [(place[widest] + 1) % result.shape[widest]] + place[widest + 1:]
    return result.at[tuple(place)].set(smallest).at[tuple(beside)].set(high)


def shard_levels(rng, extent, shards, least, top_value):
    loudness = 1.0
    for axis_at, parts in shards:
        steps = jax.random.uniform(jax.random.fold_in(jax.random.fold_in(rng, 6), axis_at), (parts,), jnp.float32, least / len(shards), top_value / len(shards))
        loudness = loudness * jnp.repeat(jnp.exp(steps), extent[axis_at] // parts).reshape((-1,) + (1,) * (len(extent) - 1 - axis_at))
    return loudness


def cumulative_ranks(count, slope):
    weights = [(1 << 20) // math.isqrt(standing ** slope) + 1 for standing in range(1, count + 1)]
    deviation = 1 + sum(weights) // (1 << 30)
    return np.cumsum(np.array([max(1, weight // deviation) for weight in weights]))


def ranked(rng, dims, number_of, slope):
    table = cumulative_ranks(number_of, slope)
    lot = jax.random.randint(jax.random.fold_in(rng, 1), dims, 0, int(table[number_of - 1]))
    standing = jnp.searchsorted(jnp.asarray(table, jnp.int32), lot, side="right")
    return jax.random.permutation(jax.random.fold_in(rng, 2), number_of)[standing].astype(jnp.int32)


def centred(own_key, extent, width, reach, shards=(), held_as=jnp.bfloat16):
    values = jax.random.normal(own_key, extent, jnp.float32) * width
    if len(shards) > 0:
        values = shard_levels(own_key, extent, shards, -0.22, 0.18) * values
    return jnp.clip(values, min=-reach, max=reach).astype(held_as)


def setup_inputs(seed: int = 0) -> dict:
    seeds = jax.random.split(jax.random.key(seed), 10)
    return {
        "pair_mult": centred(seeds[0], (PAIRS, NC), 0.25, 1.5, ((0, 256),)),
        "pair_dens": centred(seeds[1], (PAIRS,), 0.5, 3.0, ((0, 256),), jnp.float32),
        "pair_live": place_ends((jax.random.randint(seeds[2], (PAIRS,), 0, 4) < 3).astype(jnp.int32), jax.random.fold_in(seeds[2], 1), 0, 1),
        "pair_box": place_ends(ranked(seeds[3], (PAIRS,), NEAR, 2), jax.random.fold_in(seeds[3], 3), 0, NEAR - 1).astype(jnp.int32),
        "inter_mask": place_ends((jax.random.randint(seeds[4], (NBZ, NBX, NBY, OFFS), 0, 4) < 3).astype(jnp.int32), jax.random.fold_in(seeds[4], 1), 0, 1),
        "row_scale": jnp.clip(jnp.exp(jax.random.uniform(seeds[5], (OFFS, NC), jnp.float32, math.log(0.3), math.log(1.5))), 0.3, 1.5),
        "col_scale": jnp.clip(jnp.exp(jax.random.uniform(seeds[6], (OFFS, NC), jnp.float32, math.log(0.3), math.log(1.5))), 0.3, 1.5),
        "base": centred(seeds[7], (NC, NC), (NC * OFFS) ** -0.5, 0.0390625),
        "lattice": centred(seeds[8], (NC, NC), (NC * NBX * NBY * NBZ) ** -0.5, 0.0009765625, (), jnp.float32),
    }


def offset_table():
    listed = []
    for shift_z in range(-2, 3):
        for shift_x in range(-2, 3):
            for shift_y in range(-2, 3):
                if max(abs(shift_z), abs(shift_x), abs(shift_y)) == 2:
                    listed.append((shift_z, shift_x, shift_y))
    return listed


def reference(pair_mult, pair_dens, pair_live, pair_box, inter_mask, row_scale, col_scale, base, lattice):
    weighted = ((pair_dens * pair_live.astype(jnp.float32))[:, None] * pair_mult.astype(jnp.float32)).astype(jnp.bfloat16)
    device = jnp.arange(PAIRS, dtype=jnp.int32) // PAIR_DEV
    row_index = device // (N_BX * N_BY)
    slab_x = (device // N_BY) % N_BX
    slab_y = device % N_BY
    level = (row_index * BZL + pair_box // (BXL * BYL) - 2) % NBZ
    xpos = slab_x * BXL + (pair_box // BYL) % BXL
    ypos = slab_y * BYL + pair_box % BYL
    box_id = ((level * NBX + xpos) * NBY + ypos).astype(jnp.int32)
    weighted_wide = weighted.astype(jnp.float32)
    moments = jax.ops.segment_sum(weighted_wide, box_id, NBZ * NBX * NBY)
    cell = jnp.sum(weighted_wide, 0)
    stored = moments.reshape(NBZ, NBX, NBY, NC)
    far = jnp.zeros((NBZ, NBX, NBY, NC), jnp.float32)
    for entry, shifts in enumerate(offset_table()):
        source = jnp.roll(stored, (-shifts[0], -shifts[1], -shifts[2]), (0, 1, 2))
        gate_values = inter_mask[..., entry].astype(jnp.float32)[..., None]
        scaled = (source * gate_values * row_scale[entry]).astype(jnp.bfloat16)
        product = jnp.dot(scaled.reshape(-1, NC), base, preferred_element_type=jnp.float32)
        far = far + product.reshape(NBZ, NBX, NBY, NC) * col_scale[entry]
    lattice_term = jnp.dot(cell, lattice, precision=lax.Precision.HIGHEST)
    box_locals = (far + lattice_term).astype(jnp.bfloat16)
    flat_locals = box_locals.reshape(-1, NC)

    def pair_block(packed):
        mult_block, id_block = packed
        picked = flat_locals[id_block].astype(jnp.float32)
        return jnp.sum(mult_block.astype(jnp.float32) * picked, -1)

    pair_j = lax.map(pair_block, (pair_mult.reshape(DEVICES, PAIR_DEV, NC), box_id.reshape(DEVICES, PAIR_DEV)))
    return box_locals, pair_j.reshape(PAIRS)
```

```python
import numpy as np
import jax
import jax.numpy as jnp
from jax import lax
from jax.experimental import pallas as pl
from jax.experimental.pallas import tpu as pltpu
from jax.sharding import PartitionSpec as P


def padded_2(x, sides, width):
    for axis, dim in sides:
        count, length = (lax.axis_size(axis), x.shape[dim])
        up = [(i, (i + 1) % count) for i in range(count)]
        down = [(j, i) for i, j in up]
        last = lax.slice_in_dim(x, length - width, length, axis=dim)
        leading = lax.slice_in_dim(x, 0, width, axis=dim)
        before = lax.ppermute(last, axis, up)
        after = lax.ppermute(leading, axis, down)
        x = jnp.concatenate([before, x, after], axis=dim)
    return x


def offset_table():
    listed = []
    for shift_z in range(-2, 3):
        for shift_x in range(-2, 3):
            for shift_y in range(-2, 3):
                if max(abs(shift_z), abs(shift_x), abs(shift_y)) == 2:
                    listed.append((shift_z, shift_x, shift_y))
    return listed


def axis_sum(x, axis):
    count = lax.axis_size(axis)
    stride = 1
    while stride < count:
        group = min(4, count // stride)
        span = stride * group
        total = x
        for k in range(1, group):
            pairs = []
            for i in range(count):
                block, rest = divmod(i, span)
                pairs.append((i, block * span + (rest + k * stride) % span))
            total = total + lax.ppermute(x, axis, pairs)
        x = total
        stride = span
    return x


def far_kernel(tab_ref, ysh_ref, mask_ref, rs_ref, cs_ref, base_ref, lat_ref, out_ref, acc_ref):
    rows = acc_ref.shape[0]
    lanes = mask_ref.shape[1]
    acc_ref[...] = jnp.zeros(acc_ref.shape, jnp.float32)
    lane = lax.broadcasted_iota(jnp.int32, (rows, lanes), 1)

    def body(o, carry):
        a = tab_ref[3 * o]
        b = tab_ref[3 * o + 1]
        c = tab_ref[3 * o + 2]
        win = ysh_ref[c, pl.ds(a, 8), pl.ds(b, 8), :, :].reshape(rows, -1)
        gate = jnp.sum(jnp.where(lane == o, mask_ref[...], 0.0), axis=1, keepdims=True)
        scaled = (win * gate * rs_ref[pl.ds(o, 1), :]).astype(jnp.bfloat16)
        product = jnp.dot(scaled, base_ref[...], preferred_element_type=jnp.float32)
        acc_ref[...] += product * cs_ref[pl.ds(o, 1), :]
        return carry

    lax.fori_loop(0, tab_ref.shape[0] // 3, body, 0)
    out_ref[...] = (acc_ref[...] + lat_ref[...]).astype(out_ref.dtype)


def far_field(ysh, masks, row_scale, col_scale, base, lattice_term):
    rows = masks.shape[0]
    components = base.shape[1]
    table = np.array([[a + 2, b + 2, c + 2] for a, b, c in offset_table()], np.int32).reshape(-1)
    vmem = pltpu.MemorySpace.VMEM if hasattr(pltpu, "MemorySpace") else pltpu.VMEM
    smem = pltpu.MemorySpace.SMEM if hasattr(pltpu, "MemorySpace") else pltpu.SMEM
    return pl.pallas_call(
        far_kernel,
        out_shape=jax.ShapeDtypeStruct((rows, components), jnp.bfloat16),
        in_specs=[pl.BlockSpec(memory_space=smem)] + [pl.BlockSpec(memory_space=vmem)] * 6,
        out_specs=pl.BlockSpec(memory_space=vmem),
        scratch_shapes=[pltpu.VMEM((rows, components), jnp.float32)],
        compiler_params=pltpu.CompilerParams(vmem_limit_bytes=48 * 1024 * 1024),
    )(jnp.asarray(table), ysh, masks, row_scale, col_scale, base, lattice_term.reshape(1, components))


def per_device(
    pair_mult, pair_dens, pair_live, pair_box, inter_mask, row_scale, col_scale, base, lattice
):
    components = pair_mult.shape[1]
    depth, width_x, width_y, offsets = inter_mask.shape
    near_boxes = (depth + 4) * width_x * width_y
    weighted = (
        (pair_dens * pair_live.astype(jnp.float32))[:, None] * pair_mult.astype(jnp.float32)
    ).astype(jnp.bfloat16)
    cell_part = jnp.sum(weighted.astype(jnp.float32), 0)
    cell = axis_sum(axis_sum(axis_sum(cell_part, "by"), "bx"), "rows")
    lattice_term = jnp.dot(cell, lattice, precision=lax.Precision.HIGHEST)
    labels = lax.iota(jnp.int32, near_boxes)
    selector = (labels[:, None] == pair_box[None, :]).astype(jnp.bfloat16)
    partial_near = jnp.dot(selector, weighted, preferred_element_type=jnp.float32)
    partial_near = partial_near.reshape(depth + 4, width_x, width_y, components)
    bordered = padded_2(partial_near, (("rows", 0),), 2)
    stored = partial_near[2 : 2 + depth]
    stored = stored.at[:2].add(bordered[:2])
    stored = stored.at[depth - 2 :].add(bordered[depth + 6 :])
    padded = padded_2(stored, (("rows", 0), ("bx", 1), ("by", 2)), 2)
    ysh = jnp.stack([padded[:, :, c : c + width_y] for c in range(5)])
    masks = inter_mask.reshape(depth * width_x * width_y, offsets).astype(jnp.float32)
    far = far_field(ysh, masks, row_scale, col_scale, base, lattice_term)
    box_locals = far.reshape(depth, width_x, width_y, components)
    near_locals = padded_2(box_locals, (("rows", 0),), 2)
    flat_locals = near_locals.reshape(near_boxes, components)
    onehot = (pair_box[:, None] == labels[None, :]).astype(jnp.bfloat16)
    picked_rows = jnp.dot(onehot, flat_locals, preferred_element_type=jnp.float32)
    pair_j = jnp.sum(pair_mult.astype(jnp.float32) * picked_rows, -1)
    return (box_locals, pair_j)


def solution(mesh):
    return jax.shard_map(
        per_device,
        mesh=mesh,
        in_specs=(
            P(("rows", "bx", "by"), None),
            P(("rows", "bx", "by")),
            P(("rows", "bx", "by")),
            P(("rows", "bx", "by")),
            P("rows", "bx", "by", None),
            P(),
            P(),
            P(),
            P(),
        ),
        out_specs=(P("rows", "bx", "by", None), P(("rows", "bx", "by"))),
        check_vma=False,
    )
```

```python
import numpy as np
import jax
import jax.numpy as jnp
from jax import lax
from jax.experimental import pallas as pl
from jax.experimental.pallas import tpu as pltpu
from jax.sharding import PartitionSpec as P


def padded_2(x, sides, width):
    for axis, dim in sides:
        count, length = (lax.axis_size(axis), x.shape[dim])
        up = [(i, (i + 1) % count) for i in range(count)]
        down = [(j, i) for i, j in up]
        last = lax.slice_in_dim(x, length - width, length, axis=dim)
        leading = lax.slice_in_dim(x, 0, width, axis=dim)
        before = lax.ppermute(last, axis, up)
        after = lax.ppermute(leading, axis, down)
        x = jnp.concatenate([before, x, after], axis=dim)
    return x


def offset_table():
    listed = []
    for shift_z in range(-2, 3):
        for shift_x in range(-2, 3):
            for shift_y in range(-2, 3):
                if max(abs(shift_z), abs(shift_x), abs(shift_y)) == 2:
                    listed.append((shift_z, shift_x, shift_y))
    return listed


def axis_sum(x, axis):
    count = lax.axis_size(axis)
    stride = 1
    while stride < count:
        group = min(4, count // stride)
        span = stride * group
        total = x
        for k in range(1, group):
            pairs = []
            for i in range(count):
                block, rest = divmod(i, span)
                pairs.append((i, block * span + (rest + k * stride) % span))
            total = total + lax.ppermute(x, axis, pairs)
        x = total
        stride = span
    return x


def far_kernel(tab_ref, ysh_ref, mask_ref, rs_ref, cs_ref, base_ref, lat_ref, out_ref, acc_ref):
    rows = acc_ref.shape[0]
    lanes = mask_ref.shape[1]
    levels = 2
    chunk = levels * 8 * ysh_ref.shape[3]
    acc_ref[...] = jnp.zeros(acc_ref.shape, jnp.float32)
    lane = lax.broadcasted_iota(jnp.int32, (chunk, lanes), 1)

    def body(o, carry):
        a = tab_ref[3 * o]
        b = tab_ref[3 * o + 1]
        c = tab_ref[3 * o + 2]
        row_scale = rs_ref[pl.ds(o, 1), :]
        col_scale = cs_ref[pl.ds(o, 1), :]
        for q in range(rows // chunk):
            win = ysh_ref[c, pl.ds(a + levels * q, levels), pl.ds(b, 8), :, :].reshape(chunk, -1)
            gate = jnp.sum(
                jnp.where(lane == o, mask_ref[q * chunk : (q + 1) * chunk, :], 0.0), axis=1, keepdims=True
            )
            scaled = (win * gate * row_scale).astype(jnp.bfloat16)
            product = jnp.dot(scaled, base_ref[...], preferred_element_type=jnp.float32)
            acc_ref[q * chunk : (q + 1) * chunk, :] += product * col_scale
        return carry

    lax.fori_loop(0, tab_ref.shape[0] // 3, body, 0, unroll=2)
    out_ref[...] = (acc_ref[...] + lat_ref[...]).astype(out_ref.dtype)


def far_field(ysh, masks, row_scale, col_scale, base, lattice_term):
    rows = masks.shape[0]
    components = base.shape[1]
    table = np.array([[a + 2, b + 2, c + 2] for a, b, c in offset_table()], np.int32).reshape(-1)
    vmem = pltpu.MemorySpace.VMEM if hasattr(pltpu, "MemorySpace") else pltpu.VMEM
    smem = pltpu.MemorySpace.SMEM if hasattr(pltpu, "MemorySpace") else pltpu.SMEM
    return pl.pallas_call(
        far_kernel,
        out_shape=jax.ShapeDtypeStruct((rows, components), jnp.bfloat16),
        in_specs=[pl.BlockSpec(memory_space=smem)] + [pl.BlockSpec(memory_space=vmem)] * 6,
        out_specs=pl.BlockSpec(memory_space=vmem),
        scratch_shapes=[pltpu.VMEM((rows, components), jnp.float32)],
        compiler_params=pltpu.CompilerParams(vmem_limit_bytes=48 * 1024 * 1024),
    )(jnp.asarray(table), ysh, masks, row_scale, col_scale, base, lattice_term.reshape(1, components))


def per_device(
    pair_mult, pair_dens, pair_live, pair_box, inter_mask, row_scale, col_scale, base, lattice
):
    components = pair_mult.shape[1]
    depth, width_x, width_y, offsets = inter_mask.shape
    near_boxes = (depth + 4) * width_x * width_y
    weighted = (
        (pair_dens * pair_live.astype(jnp.float32))[:, None] * pair_mult.astype(jnp.float32)
    ).astype(jnp.bfloat16)
    cell_part = jnp.sum(weighted.astype(jnp.float32), 0)
    cell = axis_sum(axis_sum(axis_sum(cell_part, "by"), "bx"), "rows")
    lattice_term = jnp.dot(cell, lattice, precision=lax.Precision.HIGHEST)
    labels = lax.iota(jnp.int32, near_boxes)
    selector = (labels[:, None] == pair_box[None, :]).astype(jnp.bfloat16)
    partial_near = jnp.dot(selector, weighted, preferred_element_type=jnp.float32)
    partial_near = partial_near.reshape(depth + 4, width_x, width_y, components)
    count = lax.axis_size("rows")
    up = [(i, (i + 1) % count) for i in range(count)]
    down = [(j, i) for i, j in up]
    from_below = lax.ppermute(partial_near[depth:], "rows", up)
    from_above = lax.ppermute(partial_near[:4], "rows", down)
    zpad = partial_near.at[:4].add(from_below).at[depth:].add(from_above)
    padded = padded_2(zpad, (("bx", 1), ("by", 2)), 2)
    ysh = jnp.stack([padded[:, :, c : c + width_y] for c in range(5)])
    masks = inter_mask.reshape(depth * width_x * width_y, offsets).astype(jnp.float32)
    far = far_field(ysh, masks, row_scale, col_scale, base, lattice_term)
    box_locals = far.reshape(depth, width_x, width_y, components)
    near_locals = padded_2(box_locals, (("rows", 0),), 2)
    flat_locals = near_locals.reshape(near_boxes, components)
    onehot = (pair_box[:, None] == labels[None, :]).astype(jnp.bfloat16)
    picked_rows = jnp.dot(onehot, flat_locals, preferred_element_type=jnp.float32)
    pair_j = jnp.sum(pair_mult.astype(jnp.float32) * picked_rows, -1)
    return (box_locals, pair_j)


def solution(mesh):
    return jax.shard_map(
        per_device,
        mesh=mesh,
        in_specs=(
            P(("rows", "bx", "by"), None),
            P(("rows", "bx", "by")),
            P(("rows", "bx", "by")),
            P(("rows", "bx", "by")),
            P("rows", "bx", "by", None),
            P(),
            P(),
            P(),
            P(),
        ),
        out_specs=(P("rows", "bx", "by", None), P(("rows", "bx", "by"))),
        check_vma=False,
    )
```

```python
import numpy as np
import jax
import jax.numpy as jnp
from jax import lax
from jax.experimental import pallas as pl
from jax.experimental.pallas import tpu as pltpu
from jax.sharding import PartitionSpec as P


def padded_2(x, sides, width):
    for axis, dim in sides:
        count, length = (lax.axis_size(axis), x.shape[dim])
        up = [(i, (i + 1) % count) for i in range(count)]
        down = [(j, i) for i, j in up]
        last = lax.slice_in_dim(x, length - width, length, axis=dim)
        leading = lax.slice_in_dim(x, 0, width, axis=dim)
        before = lax.ppermute(last, axis, up)
        after = lax.ppermute(leading, axis, down)
        x = jnp.concatenate([before, x, after], axis=dim)
    return x


def offset_table():
    listed = []
    for shift_z in range(-2, 3):
        for shift_x in range(-2, 3):
            for shift_y in range(-2, 3):
                if max(abs(shift_z), abs(shift_x), abs(shift_y)) == 2:
                    listed.append((shift_z, shift_x, shift_y))
    return listed


def axis_sum(x, axis):
    count = lax.axis_size(axis)
    stride = 1
    while stride < count:
        group = min(4, count // stride)
        span = stride * group
        total = x
        for k in range(1, group):
            pairs = []
            for i in range(count):
                block, rest = divmod(i, span)
                pairs.append((i, block * span + (rest + k * stride) % span))
            total = total + lax.ppermute(x, axis, pairs)
        x = total
        stride = span
    return x


def far_kernel(tab_ref, ysh_ref, mask_ref, rs_ref, cs_ref, base_ref, out_ref, acc_ref):
    rows = acc_ref.shape[0]
    lanes = mask_ref.shape[1]
    levels = 2
    chunk = levels * 8 * ysh_ref.shape[3]
    acc_ref[...] = jnp.zeros(acc_ref.shape, jnp.float32)
    lane = lax.broadcasted_iota(jnp.int32, (chunk, lanes), 1)

    def body(o, carry):
        a = tab_ref[3 * o]
        b = tab_ref[3 * o + 1]
        c = tab_ref[3 * o + 2]
        row_scale = rs_ref[pl.ds(o, 1), :]
        col_scale = cs_ref[pl.ds(o, 1), :]
        for q in range(rows // chunk):
            win = ysh_ref[c, pl.ds(a + levels * q, levels), pl.ds(b, 8), :, :].reshape(chunk, -1)
            gate = jnp.sum(
                jnp.where(lane == o, mask_ref[q * chunk : (q + 1) * chunk, :], 0.0), axis=1, keepdims=True
            )
            scaled = (win * gate * row_scale).astype(jnp.bfloat16)
            product = jnp.dot(scaled, base_ref[...], preferred_element_type=jnp.float32)
            acc_ref[q * chunk : (q + 1) * chunk, :] += product * col_scale
        return carry

    lax.fori_loop(0, tab_ref.shape[0] // 3, body, 0, unroll=2)
    out_ref[...] = acc_ref[...]


def far_field(ysh, masks, row_scale, col_scale, base):
    rows = masks.shape[0]
    components = base.shape[1]
    table = np.array([[a + 2, b + 2, c + 2] for a, b, c in offset_table()], np.int32).reshape(-1)
    vmem = pltpu.MemorySpace.VMEM if hasattr(pltpu, "MemorySpace") else pltpu.VMEM
    smem = pltpu.MemorySpace.SMEM if hasattr(pltpu, "MemorySpace") else pltpu.SMEM
    return pl.pallas_call(
        far_kernel,
        out_shape=jax.ShapeDtypeStruct((rows, components), jnp.float32),
        in_specs=[pl.BlockSpec(memory_space=smem)] + [pl.BlockSpec(memory_space=vmem)] * 5,
        out_specs=pl.BlockSpec(memory_space=vmem),
        scratch_shapes=[pltpu.VMEM((rows, components), jnp.float32)],
        compiler_params=pltpu.CompilerParams(vmem_limit_bytes=48 * 1024 * 1024),
    )(jnp.asarray(table), ysh, masks, row_scale, col_scale, base)


def per_device(
    pair_mult, pair_dens, pair_live, pair_box, inter_mask, row_scale, col_scale, base, lattice
):
    components = pair_mult.shape[1]
    depth, width_x, width_y, offsets = inter_mask.shape
    near_boxes = (depth + 4) * width_x * width_y
    weighted = (
        (pair_dens * pair_live.astype(jnp.float32))[:, None] * pair_mult.astype(jnp.float32)
    ).astype(jnp.bfloat16)
    cell_part = jnp.sum(weighted.astype(jnp.float32), 0)
    spread = jnp.zeros((64, components), jnp.float32).at[0].set(cell_part)
    cell = lax.psum(spread, ("rows", "bx", "by"))[0]
    lattice_term = jnp.dot(cell, lattice, precision=lax.Precision.HIGHEST)
    labels = lax.iota(jnp.int32, near_boxes)
    selector = (labels[:, None] == pair_box[None, :]).astype(jnp.bfloat16)
    partial_near = jnp.dot(selector, weighted, preferred_element_type=jnp.float32)
    partial_near = partial_near.reshape(depth + 4, width_x, width_y, components)
    count = lax.axis_size("rows")
    up = [(i, (i + 1) % count) for i in range(count)]
    down = [(j, i) for i, j in up]
    from_below = lax.ppermute(partial_near[depth:], "rows", up)
    from_above = lax.ppermute(partial_near[:4], "rows", down)
    zpad = partial_near.at[:4].add(from_below).at[depth:].add(from_above)
    padded = padded_2(zpad, (("bx", 1), ("by", 2)), 2)
    ysh = jnp.stack([padded[:, :, c : c + width_y] for c in range(5)])
    masks = inter_mask.reshape(depth * width_x * width_y, offsets).astype(jnp.float32)
    far = far_field(ysh, masks, row_scale, col_scale, base)
    box_locals = (far + lattice_term).astype(jnp.bfloat16).reshape(depth, width_x, width_y, components)
    near_locals = padded_2(box_locals, (("rows", 0),), 2)
    flat_locals = near_locals.reshape(near_boxes, components)
    onehot = (pair_box[:, None] == labels[None, :]).astype(jnp.bfloat16)
    picked_rows = jnp.dot(onehot, flat_locals, preferred_element_type=jnp.float32)
    pair_j = jnp.sum(pair_mult.astype(jnp.float32) * picked_rows, -1)
    return (box_locals, pair_j)


def solution(mesh):
    return jax.shard_map(
        per_device,
        mesh=mesh,
        in_specs=(
            P(("rows", "bx", "by"), None),
            P(("rows", "bx", "by")),
            P(("rows", "bx", "by")),
            P(("rows", "bx", "by")),
            P("rows", "bx", "by", None),
            P(),
            P(),
            P(),
            P(),
        ),
        out_specs=(P("rows", "bx", "by", None), P(("rows", "bx", "by"))),
        check_vma=False,
    )
```

```python
import functools

import numpy as np
import jax
import jax.numpy as jnp
from jax import lax
from jax.experimental import pallas as pl
from jax.experimental.pallas import tpu as pltpu
from jax.sharding import PartitionSpec as P


def padded_2(x, sides, width):
    for axis, dim in sides:
        count, length = (lax.axis_size(axis), x.shape[dim])
        up = [(i, (i + 1) % count) for i in range(count)]
        down = [(j, i) for i, j in up]
        last = lax.slice_in_dim(x, length - width, length, axis=dim)
        leading = lax.slice_in_dim(x, 0, width, axis=dim)
        before = lax.ppermute(last, axis, up)
        after = lax.ppermute(leading, axis, down)
        x = jnp.concatenate([before, x, after], axis=dim)
    return x


def offset_table():
    listed = []
    for shift_z in range(-2, 3):
        for shift_x in range(-2, 3):
            for shift_y in range(-2, 3):
                if max(abs(shift_z), abs(shift_x), abs(shift_y)) == 2:
                    listed.append((shift_z, shift_x, shift_y))
    return listed


def sum_rounds(axes):
    rounds = []
    for axis in axes:
        count = lax.axis_size(axis)
        stride = 1
        while stride < count:
            group = min(4, count // stride)
            span = stride * group
            shifts = []
            for k in range(1, group):
                pairs = []
                for i in range(count):
                    block, rest = divmod(i, span)
                    pairs.append((i, block * span + (rest + k * stride) % span))
                shifts.append(pairs)
            rounds.append((axis, shifts))
            stride = span
    return rounds


def sum_round(x, step):
    axis, shifts = step
    total = x
    for pairs in shifts:
        total = total + lax.ppermute(x, axis, pairs)
    return total


def far_kernel(first, last, tab_ref, ysh_ref, mask_ref, rs_ref, cs_ref, base_ref, init_ref, out_ref):
    rows = out_ref.shape[0]
    acc_ref = out_ref
    lanes = mask_ref.shape[1]
    levels = 2
    chunk = levels * 8 * ysh_ref.shape[3]
    acc_ref[...] = init_ref[...]
    lane = lax.broadcasted_iota(jnp.int32, (chunk, lanes), 1)

    def body(o, carry):
        a = tab_ref[3 * o]
        b = tab_ref[3 * o + 1]
        c = tab_ref[3 * o + 2]
        row_scale = rs_ref[pl.ds(o, 1), :]
        col_scale = cs_ref[pl.ds(o, 1), :]
        for q in range(rows // chunk):
            win = ysh_ref[c, pl.ds(a + levels * q, levels), pl.ds(b, 8), :, :].reshape(chunk, -1)
            gate = jnp.sum(
                jnp.where(lane == o, mask_ref[q * chunk : (q + 1) * chunk, :], 0.0), axis=1, keepdims=True
            )
            scaled = (win * gate * row_scale).astype(jnp.bfloat16)
            product = jnp.dot(scaled, base_ref[...], preferred_element_type=jnp.float32)
            acc_ref[q * chunk : (q + 1) * chunk, :] += product * col_scale
        return carry

    lax.fori_loop(first, last, body, 0, unroll=2)


def far_field(first, last, ysh, masks, row_scale, col_scale, base, acc):
    rows = masks.shape[0]
    components = base.shape[1]
    table = np.array([[a + 2, b + 2, c + 2] for a, b, c in offset_table()], np.int32).reshape(-1)
    vmem = pltpu.MemorySpace.VMEM if hasattr(pltpu, "MemorySpace") else pltpu.VMEM
    smem = pltpu.MemorySpace.SMEM if hasattr(pltpu, "MemorySpace") else pltpu.SMEM
    return pl.pallas_call(
        functools.partial(far_kernel, first, last),
        out_shape=jax.ShapeDtypeStruct((rows, components), jnp.float32),
        in_specs=[pl.BlockSpec(memory_space=smem)] + [pl.BlockSpec(memory_space=vmem)] * 6,
        out_specs=pl.BlockSpec(memory_space=vmem),
        compiler_params=pltpu.CompilerParams(vmem_limit_bytes=48 * 1024 * 1024),
    )(jnp.asarray(table), ysh, masks, row_scale, col_scale, base, acc)


def per_device(
    pair_mult, pair_dens, pair_live, pair_box, inter_mask, row_scale, col_scale, base, lattice
):
    components = pair_mult.shape[1]
    depth, width_x, width_y, offsets = inter_mask.shape
    near_boxes = (depth + 4) * width_x * width_y
    weighted = (
        (pair_dens * pair_live.astype(jnp.float32))[:, None] * pair_mult.astype(jnp.float32)
    ).astype(jnp.bfloat16)
    cell_part = jnp.sum(weighted.astype(jnp.float32), 0)
    labels = lax.iota(jnp.int32, near_boxes)
    selector = (labels[:, None] == pair_box[None, :]).astype(jnp.bfloat16)
    partial_near = jnp.dot(selector, weighted, preferred_element_type=jnp.float32)
    partial_near = partial_near.reshape(depth + 4, width_x, width_y, components)
    count = lax.axis_size("rows")
    up = [(i, (i + 1) % count) for i in range(count)]
    down = [(j, i) for i, j in up]
    from_below = lax.ppermute(partial_near[depth:], "rows", up)
    from_above = lax.ppermute(partial_near[:4], "rows", down)
    zpad = partial_near.at[:4].add(from_below).at[depth:].add(from_above)
    padded = padded_2(zpad, (("bx", 1), ("by", 2)), 2)
    ysh = jnp.stack([padded[:, :, c : c + width_y] for c in range(5)])
    masks = inter_mask.reshape(depth * width_x * width_y, offsets).astype(jnp.float32)
    rounds = sum_rounds(("by", "bx", "rows"))
    bounds = np.linspace(0, offsets, len(rounds) + 1).round().astype(int)
    cell = cell_part
    far = jnp.zeros((depth * width_x * width_y, components), jnp.float32)
    for step, first, last in zip(rounds, bounds[:-1], bounds[1:]):
        cell = sum_round(cell, step)
        far = far_field(int(first), int(last), ysh, masks, row_scale, col_scale, base, far)
        cell, far = lax.optimization_barrier((cell, far))
    lattice_term = jnp.dot(cell, lattice, precision=lax.Precision.HIGHEST)
    box_locals = (far + lattice_term).astype(jnp.bfloat16).reshape(depth, width_x, width_y, components)
    near_locals = padded_2(box_locals, (("rows", 0),), 2)
    flat_locals = near_locals.reshape(near_boxes, components)
    onehot = (pair_box[:, None] == labels[None, :]).astype(jnp.bfloat16)
    picked_rows = jnp.dot(onehot, flat_locals, preferred_element_type=jnp.float32)
    pair_j = jnp.sum(pair_mult.astype(jnp.float32) * picked_rows, -1)
    return (box_locals, pair_j)


def solution(mesh):
    return jax.shard_map(
        per_device,
        mesh=mesh,
        in_specs=(
            P(("rows", "bx", "by"), None),
            P(("rows", "bx", "by")),
            P(("rows", "bx", "by")),
            P(("rows", "bx", "by")),
            P("rows", "bx", "by", None),
            P(),
            P(),
            P(),
            P(),
        ),
        out_specs=(P("rows", "bx", "by", None), P(("rows", "bx", "by"))),
        check_vma=False,
    )
```

```python
import numpy as np
import jax
import jax.numpy as jnp
from jax import lax
from jax.experimental import pallas as pl
from jax.experimental.pallas import tpu as pltpu
from jax.sharding import PartitionSpec as P


def padded_2(x, sides, width):
    for axis, dim in sides:
        count, length = (lax.axis_size(axis), x.shape[dim])
        up = [(i, (i + 1) % count) for i in range(count)]
        down = [(j, i) for i, j in up]
        last = lax.slice_in_dim(x, length - width, length, axis=dim)
        leading = lax.slice_in_dim(x, 0, width, axis=dim)
        before = lax.ppermute(last, axis, up)
        after = lax.ppermute(leading, axis, down)
        x = jnp.concatenate([before, x, after], axis=dim)
    return x


def offset_table():
    listed = []
    for shift_z in range(-2, 3):
        for shift_x in range(-2, 3):
            for shift_y in range(-2, 3):
                if max(abs(shift_z), abs(shift_x), abs(shift_y)) == 2:
                    listed.append((shift_z, shift_x, shift_y))
    return listed


def axis_sum(x, axis):
    count = lax.axis_size(axis)
    bit = 1
    while bit < count:
        x = x + lax.ppermute(x, axis, [(i, i ^ bit) for i in range(count)])
        bit *= 2
    return x


def far_kernel(tab_ref, ysh_ref, mask_ref, rs_ref, cs_ref, base_ref, lat_ref, out_ref, acc_ref):
    rows = acc_ref.shape[0]
    lanes = mask_ref.shape[1]
    levels = 2
    chunk = levels * 8 * ysh_ref.shape[3]
    acc_ref[...] = jnp.zeros(acc_ref.shape, jnp.float32)
    lane = lax.broadcasted_iota(jnp.int32, (chunk, lanes), 1)

    def body(o, carry):
        a = tab_ref[3 * o]
        b = tab_ref[3 * o + 1]
        c = tab_ref[3 * o + 2]
        row_scale = rs_ref[pl.ds(o, 1), :]
        col_scale = cs_ref[pl.ds(o, 1), :]
        for q in range(rows // chunk):
            win = ysh_ref[c, pl.ds(a + levels * q, levels), pl.ds(b, 8), :, :].reshape(chunk, -1)
            gate = jnp.sum(
                jnp.where(lane == o, mask_ref[q * chunk : (q + 1) * chunk, :], 0.0), axis=1, keepdims=True
            )
            scaled = (win * gate * row_scale).astype(jnp.bfloat16)
            product = jnp.dot(scaled, base_ref[...], preferred_element_type=jnp.float32)
            acc_ref[q * chunk : (q + 1) * chunk, :] += product * col_scale
        return carry

    lax.fori_loop(0, tab_ref.shape[0] // 3, body, 0, unroll=2)
    out_ref[...] = (acc_ref[...] + lat_ref[...]).astype(out_ref.dtype)


def far_field(ysh, masks, row_scale, col_scale, base, lattice_term):
    rows = masks.shape[0]
    components = base.shape[1]
    table = np.array([[a + 2, b + 2, c + 2] for a, b, c in offset_table()], np.int32).reshape(-1)
    vmem = pltpu.MemorySpace.VMEM if hasattr(pltpu, "MemorySpace") else pltpu.VMEM
    smem = pltpu.MemorySpace.SMEM if hasattr(pltpu, "MemorySpace") else pltpu.SMEM
    return pl.pallas_call(
        far_kernel,
        out_shape=jax.ShapeDtypeStruct((rows, components), jnp.bfloat16),
        in_specs=[pl.BlockSpec(memory_space=smem)] + [pl.BlockSpec(memory_space=vmem)] * 6,
        out_specs=pl.BlockSpec(memory_space=vmem),
        scratch_shapes=[pltpu.VMEM((rows, components), jnp.float32)],
        compiler_params=pltpu.CompilerParams(vmem_limit_bytes=48 * 1024 * 1024),
    )(jnp.asarray(table), ysh, masks, row_scale, col_scale, base, lattice_term.reshape(1, components))


def per_device(
    pair_mult, pair_dens, pair_live, pair_box, inter_mask, row_scale, col_scale, base, lattice
):
    components = pair_mult.shape[1]
    depth, width_x, width_y, offsets = inter_mask.shape
    near_boxes = (depth + 4) * width_x * width_y
    weighted = (
        (pair_dens * pair_live.astype(jnp.float32))[:, None] * pair_mult.astype(jnp.float32)
    ).astype(jnp.bfloat16)
    cell_part = jnp.sum(weighted.astype(jnp.float32), 0)
    cell = axis_sum(axis_sum(axis_sum(cell_part, "by"), "bx"), "rows")
    lattice_term = jnp.dot(cell, lattice, precision=lax.Precision.HIGHEST)
    labels = lax.iota(jnp.int32, near_boxes)
    selector = (labels[:, None] == pair_box[None, :]).astype(jnp.bfloat16)
    partial_near = jnp.dot(selector, weighted, preferred_element_type=jnp.float32)
    partial_near = partial_near.reshape(depth + 4, width_x, width_y, components)
    count = lax.axis_size("rows")
    up = [(i, (i + 1) % count) for i in range(count)]
    down = [(j, i) for i, j in up]
    from_below = lax.ppermute(partial_near[depth:], "rows", up)
    from_above = lax.ppermute(partial_near[:4], "rows", down)
    zpad = partial_near.at[:4].add(from_below).at[depth:].add(from_above)
    padded = padded_2(zpad, (("bx", 1), ("by", 2)), 2)
    ysh = jnp.stack([padded[:, :, c : c + width_y] for c in range(5)])
    masks = inter_mask.reshape(depth * width_x * width_y, offsets).astype(jnp.float32)
    far = far_field(ysh, masks, row_scale, col_scale, base, lattice_term)
    box_locals = far.reshape(depth, width_x, width_y, components)
    near_locals = padded_2(box_locals, (("rows", 0),), 2)
    flat_locals = near_locals.reshape(near_boxes, components)
    onehot = (pair_box[:, None] == labels[None, :]).astype(jnp.bfloat16)
    picked_rows = jnp.dot(onehot, flat_locals, preferred_element_type=jnp.float32)
    pair_j = jnp.sum(pair_mult.astype(jnp.float32) * picked_rows, -1)
    return (box_locals, pair_j)


def solution(mesh):
    return jax.shard_map(
        per_device,
        mesh=mesh,
        in_specs=(
            P(("rows", "bx", "by"), None),
            P(("rows", "bx", "by")),
            P(("rows", "bx", "by")),
            P(("rows", "bx", "by")),
            P("rows", "bx", "by", None),
            P(),
            P(),
            P(),
            P(),
        ),
        out_specs=(P("rows", "bx", "by", None), P(("rows", "bx", "by"))),
        check_vma=False,
    )
```

```python
import numpy as np
import jax
import jax.numpy as jnp
from jax import lax
from jax.experimental import pallas as pl
from jax.experimental.pallas import tpu as pltpu
from jax.sharding import PartitionSpec as P


def padded_2(x, sides, width):
    for axis, dim in sides:
        count, length = (lax.axis_size(axis), x.shape[dim])
        up = [(i, (i + 1) % count) for i in range(count)]
        down = [(j, i) for i, j in up]
        last = lax.slice_in_dim(x, length - width, length, axis=dim)
        leading = lax.slice_in_dim(x, 0, width, axis=dim)
        before = lax.ppermute(last, axis, up)
        after = lax.ppermute(leading, axis, down)
        x = jnp.concatenate([before, x, after], axis=dim)
    return x


def offset_table():
    listed = []
    for shift_z in range(-2, 3):
        for shift_x in range(-2, 3):
            for shift_y in range(-2, 3):
                if max(abs(shift_z), abs(shift_x), abs(shift_y)) == 2:
                    listed.append((shift_z, shift_x, shift_y))
    return listed


def axis_sum(x, axis):
    count = lax.axis_size(axis)
    stride = 1
    while stride < count:
        group = min(4, count // stride)
        span = stride * group
        total = x
        for k in range(1, group):
            pairs = []
            for i in range(count):
                block, rest = divmod(i, span)
                pairs.append((i, block * span + (rest + k * stride) % span))
            total = total + lax.ppermute(x, axis, pairs)
        x = total
        stride = span
    return x


def far_kernel(tab_ref, ysh_ref, mask_ref, rs_ref, cs_ref, base_ref, lat_ref, out_ref, acc_ref):
    rows = acc_ref.shape[0]
    lanes = mask_ref.shape[1]
    levels = 2
    chunk = levels * 8 * ysh_ref.shape[3]
    acc_ref[...] = jnp.zeros(acc_ref.shape, jnp.float32)
    lane = lax.broadcasted_iota(jnp.int32, (chunk, lanes), 1)

    def body(o, carry):
        a = tab_ref[3 * o]
        b = tab_ref[3 * o + 1]
        c = tab_ref[3 * o + 2]
        row_scale = rs_ref[pl.ds(o, 1), :]
        col_scale = cs_ref[pl.ds(o, 1), :]
        for q in range(rows // chunk):
            win = ysh_ref[c, pl.ds(a + levels * q, levels), pl.ds(b, 8), :, :].reshape(chunk, -1)
            gate = jnp.sum(
                jnp.where(lane == o, mask_ref[q * chunk : (q + 1) * chunk, :], 0.0), axis=1, keepdims=True
            )
            scaled = (win * gate * row_scale).astype(jnp.bfloat16)
            product = jnp.dot(scaled, base_ref[...], preferred_element_type=jnp.float32)
            acc_ref[q * chunk : (q + 1) * chunk, :] += product * col_scale
        return carry

    lax.fori_loop(0, tab_ref.shape[0] // 3, body, 0, unroll=2)
    out_ref[...] = (acc_ref[...] + lat_ref[...]).astype(out_ref.dtype)


def far_field(ysh, masks, row_scale, col_scale, base, lattice_term):
    rows = masks.shape[0]
    components = base.shape[1]
    table = np.array([[a + 2, b + 2, c + 2] for a, b, c in offset_table()], np.int32).reshape(-1)
    vmem = pltpu.MemorySpace.VMEM if hasattr(pltpu, "MemorySpace") else pltpu.VMEM
    smem = pltpu.MemorySpace.SMEM if hasattr(pltpu, "MemorySpace") else pltpu.SMEM
    return pl.pallas_call(
        far_kernel,
        out_shape=jax.ShapeDtypeStruct((rows, components), jnp.bfloat16),
        in_specs=[pl.BlockSpec(memory_space=smem)] + [pl.BlockSpec(memory_space=vmem)] * 6,
        out_specs=pl.BlockSpec(memory_space=vmem),
        scratch_shapes=[pltpu.VMEM((rows, components), jnp.float32)],
        compiler_params=pltpu.CompilerParams(vmem_limit_bytes=48 * 1024 * 1024),
    )(jnp.asarray(table), ysh, masks, row_scale, col_scale, base, lattice_term.reshape(1, components))


def per_device(
    pair_mult, pair_dens, pair_live, pair_box, inter_mask, row_scale, col_scale, base, lattice
):
    components = pair_mult.shape[1]
    depth, width_x, width_y, offsets = inter_mask.shape
    near_boxes = (depth + 4) * width_x * width_y
    weighted = (
        (pair_dens * pair_live.astype(jnp.float32))[:, None] * pair_mult.astype(jnp.float32)
    ).astype(jnp.bfloat16)
    cell_part = jnp.sum(weighted.astype(jnp.float32), 0)
    cell = axis_sum(axis_sum(axis_sum(cell_part, "by"), "bx"), "rows")
    lattice_term = jnp.dot(cell, lattice, precision=lax.Precision.HIGHEST)
    weighted, lattice_term = lax.optimization_barrier((weighted, lattice_term))
    labels = lax.iota(jnp.int32, near_boxes)
    selector = (labels[:, None] == pair_box[None, :]).astype(jnp.bfloat16)
    partial_near = jnp.dot(selector, weighted, preferred_element_type=jnp.float32)
    partial_near = partial_near.reshape(depth + 4, width_x, width_y, components)
    count = lax.axis_size("rows")
    up = [(i, (i + 1) % count) for i in range(count)]
    down = [(j, i) for i, j in up]
    from_below = lax.ppermute(partial_near[depth:], "rows", up)
    from_above = lax.ppermute(partial_near[:4], "rows", down)
    zpad = partial_near.at[:4].add(from_below).at[depth:].add(from_above)
    padded = padded_2(zpad, (("bx", 1), ("by", 2)), 2)
    ysh = jnp.stack([padded[:, :, c : c + width_y] for c in range(5)])
    masks = inter_mask.reshape(depth * width_x * width_y, offsets).astype(jnp.float32)
    far = far_field(ysh, masks, row_scale, col_scale, base, lattice_term)
    box_locals = far.reshape(depth, width_x, width_y, components)
    near_locals = padded_2(box_locals, (("rows", 0),), 2)
    flat_locals = near_locals.reshape(near_boxes, components)
    onehot = (pair_box[:, None] == labels[None, :]).astype(jnp.bfloat16)
    picked_rows = jnp.dot(onehot, flat_locals, preferred_element_type=jnp.float32)
    pair_j = jnp.sum(pair_mult.astype(jnp.float32) * picked_rows, -1)
    return (box_locals, pair_j)


def solution(mesh):
    return jax.shard_map(
        per_device,
        mesh=mesh,
        in_specs=(
            P(("rows", "bx", "by"), None),
            P(("rows", "bx", "by")),
            P(("rows", "bx", "by")),
            P(("rows", "bx", "by")),
            P("rows", "bx", "by", None),
            P(),
            P(),
            P(),
            P(),
        ),
        out_specs=(P("rows", "bx", "by", None), P(("rows", "bx", "by"))),
        check_vma=False,
    )
```

```python
import numpy as np
import jax
import jax.numpy as jnp
from jax import lax
from jax.experimental import pallas as pl
from jax.experimental.pallas import tpu as pltpu
from jax.sharding import PartitionSpec as P


def padded_2(x, sides, width):
    for axis, dim in sides:
        count, length = (lax.axis_size(axis), x.shape[dim])
        up = [(i, (i + 1) % count) for i in range(count)]
        down = [(j, i) for i, j in up]
        last = lax.slice_in_dim(x, length - width, length, axis=dim)
        leading = lax.slice_in_dim(x, 0, width, axis=dim)
        before = lax.ppermute(last, axis, up)
        after = lax.ppermute(leading, axis, down)
        x = jnp.concatenate([before, x, after], axis=dim)
    return x


def offset_table():
    listed = []
    for shift_z in range(-2, 3):
        for shift_x in range(-2, 3):
            for shift_y in range(-2, 3):
                if max(abs(shift_z), abs(shift_x), abs(shift_y)) == 2:
                    listed.append((shift_z, shift_x, shift_y))
    return listed


def sum_rounds(axes):
    rounds = []
    for axis in axes:
        count = lax.axis_size(axis)
        stride = 1
        while stride < count:
            group = min(4, count // stride)
            span = stride * group
            shifts = []
            for k in range(1, group):
                pairs = []
                for i in range(count):
                    block, rest = divmod(i, span)
                    pairs.append((i, block * span + (rest + k * stride) % span))
                shifts.append(pairs)
            rounds.append((axis, shifts))
            stride = span
    return rounds


def sum_round(x, step):
    axis, shifts = step
    total = x
    for pairs in shifts:
        total = total + lax.ppermute(x, axis, pairs)
    return total


def far_kernel(tab_ref, ysh_ref, mask_ref, rs_ref, cs_ref, base_ref, out_ref, acc_ref):
    rows = acc_ref.shape[0]
    lanes = mask_ref.shape[1]
    levels = 2
    chunk = levels * 8 * ysh_ref.shape[3]
    acc_ref[...] = jnp.zeros(acc_ref.shape, jnp.float32)
    lane = lax.broadcasted_iota(jnp.int32, (chunk, lanes), 1)

    def body(o, carry):
        a = tab_ref[3 * o]
        b = tab_ref[3 * o + 1]
        c = tab_ref[3 * o + 2]
        row_scale = rs_ref[pl.ds(o, 1), :]
        col_scale = cs_ref[pl.ds(o, 1), :]
        for q in range(rows // chunk):
            win = ysh_ref[c, pl.ds(a + levels * q, levels), pl.ds(b, 8), :, :].reshape(chunk, -1)
            gate = jnp.sum(
                jnp.where(lane == o, mask_ref[q * chunk : (q + 1) * chunk, :], 0.0), axis=1, keepdims=True
            )
            scaled = (win * gate * row_scale).astype(jnp.bfloat16)
            product = jnp.dot(scaled, base_ref[...], preferred_element_type=jnp.float32)
            acc_ref[q * chunk : (q + 1) * chunk, :] += product * col_scale
        return carry

    lax.fori_loop(0, tab_ref.shape[0] // 3, body, 0, unroll=7)
    out_ref[...] = acc_ref[...]


def far_field(ysh, masks, row_scale, col_scale, base):
    rows = masks.shape[0]
    components = base.shape[1]
    table = np.array([[a + 2, b + 2, c + 2] for a, b, c in offset_table()], np.int32).reshape(-1)
    vmem = pltpu.MemorySpace.VMEM if hasattr(pltpu, "MemorySpace") else pltpu.VMEM
    smem = pltpu.MemorySpace.SMEM if hasattr(pltpu, "MemorySpace") else pltpu.SMEM
    return pl.pallas_call(
        far_kernel,
        out_shape=jax.ShapeDtypeStruct((rows, components), jnp.float32),
        in_specs=[pl.BlockSpec(memory_space=smem)] + [pl.BlockSpec(memory_space=vmem)] * 5,
        out_specs=pl.BlockSpec(memory_space=vmem),
        scratch_shapes=[pltpu.VMEM((rows, components), jnp.float32)],
        compiler_params=pltpu.CompilerParams(vmem_limit_bytes=48 * 1024 * 1024),
    )(jnp.asarray(table), ysh, masks, row_scale, col_scale, base)


def device_body(
    pair_mult, pair_dens, pair_live, pair_box, inter_mask, row_scale, col_scale, base, lattice
):
    components = pair_mult.shape[1]
    depth, width_x, width_y, offsets = inter_mask.shape
    near_boxes = (depth + 4) * width_x * width_y
    weighted = (
        (pair_dens * pair_live.astype(jnp.float32))[:, None] * pair_mult.astype(jnp.float32)
    ).astype(jnp.bfloat16)
    cell_part = jnp.sum(weighted.astype(jnp.float32), 0)
    rounds = sum_rounds(("by", "bx", "rows"))
    cell = sum_round(sum_round(cell_part, rounds[0]), rounds[1])
    labels = lax.iota(jnp.int32, near_boxes)
    selector = (labels[:, None] == pair_box[None, :]).astype(jnp.bfloat16)
    partial_near = jnp.dot(selector, weighted, preferred_element_type=jnp.float32)
    partial_near = partial_near.reshape(depth + 4, width_x, width_y, components)
    count = lax.axis_size("rows")
    up = [(i, (i + 1) % count) for i in range(count)]
    down = [(j, i) for i, j in up]
    from_below = lax.ppermute(partial_near[depth:], "rows", up)
    from_above = lax.ppermute(partial_near[:4], "rows", down)
    zpad = partial_near.at[:4].add(from_below).at[depth:].add(from_above)
    padded = padded_2(zpad, (("bx", 1), ("by", 2)), 2)
    ysh = jnp.stack([padded[:, :, c : c + width_y] for c in range(5)])
    masks = inter_mask.reshape(depth * width_x * width_y, offsets).astype(jnp.float32)
    cell = sum_round(cell, rounds[2])
    far = far_field(ysh, masks, row_scale, col_scale, base)
    cell, far = lax.optimization_barrier((cell, far))
    near_far = padded_2(far.reshape(depth, width_x, width_y, components), (("rows", 0),), 2)
    cell = sum_round(cell, rounds[3])
    lattice_term = jnp.dot(cell, lattice, precision=lax.Precision.HIGHEST)
    near_locals = (near_far + lattice_term).astype(jnp.bfloat16)
    box_locals = near_locals[2 : 2 + depth]
    flat_locals = near_locals.reshape(near_boxes, components)
    onehot = (pair_box[:, None] == labels[None, :]).astype(jnp.bfloat16)
    picked_rows = jnp.dot(onehot, flat_locals, preferred_element_type=jnp.float32)
    pair_j = jnp.sum(pair_mult.astype(jnp.float32) * picked_rows, -1)
    return (box_locals, pair_j)


def solution(mesh):
    return jax.shard_map(
        device_body,
        mesh=mesh,
        in_specs=(
            P(("rows", "bx", "by"), None),
            P(("rows", "bx", "by")),
            P(("rows", "bx", "by")),
            P(("rows", "bx", "by")),
            P("rows", "bx", "by", None),
            P(),
            P(),
            P(),
            P(),
        ),
        out_specs=(P("rows", "bx", "by", None), P(("rows", "bx", "by"))),
        check_vma=False,
    )
```

```python
import numpy as np
import jax
import jax.numpy as jnp
from jax import lax
from jax.experimental import pallas as pl
from jax.experimental.pallas import tpu as pltpu
from jax.sharding import PartitionSpec as P


def padded_2(x, sides, width):
    for axis, dim in sides:
        count, length = (lax.axis_size(axis), x.shape[dim])
        up = [(i, (i + 1) % count) for i in range(count)]
        down = [(j, i) for i, j in up]
        last = lax.slice_in_dim(x, length - width, length, axis=dim)
        leading = lax.slice_in_dim(x, 0, width, axis=dim)
        before = lax.ppermute(last, axis, up)
        after = lax.ppermute(leading, axis, down)
        x = jnp.concatenate([before, x, after], axis=dim)
    return x


def offset_table():
    listed = []
    for shift_z in range(-2, 3):
        for shift_x in range(-2, 3):
            for shift_y in range(-2, 3):
                if max(abs(shift_z), abs(shift_x), abs(shift_y)) == 2:
                    listed.append((shift_z, shift_x, shift_y))
    return listed


def sum_rounds(axes):
    rounds = []
    for axis in axes:
        count = lax.axis_size(axis)
        stride = 1
        while stride < count:
            group = min(4, count // stride)
            span = stride * group
            shifts = []
            for k in range(1, group):
                pairs = []
                for i in range(count):
                    block, rest = divmod(i, span)
                    pairs.append((i, block * span + (rest + k * stride) % span))
                shifts.append(pairs)
            rounds.append((axis, shifts))
            stride = span
    return rounds


def sum_round(x, step):
    axis, shifts = step
    total = x
    for pairs in shifts:
        total = total + lax.ppermute(x, axis, pairs)
    return total


def far_kernel(tab_ref, ysh_ref, mask_ref, rs_ref, cs_ref, base_ref, out_ref, acc_ref):
    rows = acc_ref.shape[0]
    lanes = mask_ref.shape[1]
    levels = 2
    chunk = levels * 8 * ysh_ref.shape[3]
    acc_ref[...] = jnp.zeros(acc_ref.shape, jnp.float32)
    lane = lax.broadcasted_iota(jnp.int32, (chunk, lanes), 1)

    def body(o, carry):
        a = tab_ref[3 * o]
        b = tab_ref[3 * o + 1]
        c = tab_ref[3 * o + 2]
        row_scale = rs_ref[pl.ds(o, 1), :]
        col_scale = cs_ref[pl.ds(o, 1), :]
        for q in range(rows // chunk):
            win = ysh_ref[c, pl.ds(a + levels * q, levels), pl.ds(b, 8), :, :].reshape(chunk, -1)
            gate = jnp.sum(
                jnp.where(lane == o, mask_ref[q * chunk : (q + 1) * chunk, :], 0.0), axis=1, keepdims=True
            )
            scaled = (win * gate * row_scale).astype(jnp.bfloat16)
            product = jnp.dot(scaled, base_ref[...], preferred_element_type=jnp.float32)
            acc_ref[q * chunk : (q + 1) * chunk, :] += product * col_scale
        return carry

    lax.fori_loop(0, tab_ref.shape[0] // 3, body, 0, unroll=7)
    out_ref[...] = acc_ref[...]


def far_field(ysh, masks, row_scale, col_scale, base):
    rows = masks.shape[0]
    components = base.shape[1]
    table = np.array([[a + 2, b + 2, c + 2] for a, b, c in offset_table()], np.int32).reshape(-1)
    vmem = pltpu.MemorySpace.VMEM if hasattr(pltpu, "MemorySpace") else pltpu.VMEM
    smem = pltpu.MemorySpace.SMEM if hasattr(pltpu, "MemorySpace") else pltpu.SMEM
    return pl.pallas_call(
        far_kernel,
        out_shape=jax.ShapeDtypeStruct((rows, components), jnp.float32),
        in_specs=[pl.BlockSpec(memory_space=smem)] + [pl.BlockSpec(memory_space=vmem)] * 5,
        out_specs=pl.BlockSpec(memory_space=vmem),
        scratch_shapes=[pltpu.VMEM((rows, components), jnp.float32)],
        compiler_params=pltpu.CompilerParams(vmem_limit_bytes=48 * 1024 * 1024),
    )(jnp.asarray(table), ysh, masks, row_scale, col_scale, base)


def device_body(
    pair_mult, pair_dens, pair_live, pair_box, inter_mask, row_scale, col_scale, base, lattice
):
    components = pair_mult.shape[1]
    depth, width_x, width_y, offsets = inter_mask.shape
    near_boxes = (depth + 4) * width_x * width_y
    weighted = (
        (pair_dens * pair_live.astype(jnp.float32))[:, None] * pair_mult.astype(jnp.float32)
    ).astype(jnp.bfloat16)
    cell_part = jnp.sum(weighted.astype(jnp.float32), 0)
    rounds = sum_rounds(("by", "bx", "rows"))
    cell = sum_round(sum_round(cell_part, rounds[0]), rounds[1])
    labels = lax.iota(jnp.int32, near_boxes)
    selector = (labels[:, None] == pair_box[None, :]).astype(jnp.bfloat16)
    partial_near = jnp.dot(selector, weighted, preferred_element_type=jnp.float32)
    partial_near = partial_near.reshape(depth + 4, width_x, width_y, components)
    count = lax.axis_size("rows")
    up = [(i, (i + 1) % count) for i in range(count)]
    down = [(j, i) for i, j in up]
    from_below = lax.ppermute(partial_near[depth:], "rows", up)
    from_above = lax.ppermute(partial_near[:4], "rows", down)
    zpad = partial_near.at[:4].add(from_below).at[depth:].add(from_above)
    padded = padded_2(zpad, (("bx", 1), ("by", 2)), 2)
    ysh = jnp.stack([padded[:, :, c : c + width_y] for c in range(5)])
    masks = inter_mask.reshape(depth * width_x * width_y, offsets).astype(jnp.float32)
    cell = sum_round(cell, rounds[2])
    far = far_field(ysh, masks, row_scale, col_scale, base)
    cell, far = lax.optimization_barrier((cell, far))
    near_far = padded_2(far.reshape(depth, width_x, width_y, components), (("rows", 0),), 2)
    cell = sum_round(cell, rounds[3])
    lattice_term = jnp.dot(cell, lattice, precision=lax.Precision.HIGHEST)
    near_locals = (near_far + lattice_term).astype(jnp.bfloat16)
    box_locals = near_locals[2 : 2 + depth]
    flat_locals = near_locals.reshape(near_boxes, components)
    onehot = (pair_box[:, None] == labels[None, :]).astype(jnp.bfloat16)
    picked_rows = jnp.dot(onehot, flat_locals, preferred_element_type=jnp.float32)
    product = pair_mult.astype(jnp.float32) * picked_rows
    high = product.astype(jnp.bfloat16)
    low = (product - high.astype(jnp.float32)).astype(jnp.bfloat16)
    ones = jnp.ones((components,), jnp.bfloat16)
    pair_j = jnp.dot(high, ones, preferred_element_type=jnp.float32) + jnp.dot(low, ones, preferred_element_type=jnp.float32)
    return (box_locals, pair_j)


def solution(mesh):
    return jax.shard_map(
        device_body,
        mesh=mesh,
        in_specs=(
            P(("rows", "bx", "by"), None),
            P(("rows", "bx", "by")),
            P(("rows", "bx", "by")),
            P(("rows", "bx", "by")),
            P("rows", "bx", "by", None),
            P(),
            P(),
            P(),
            P(),
        ),
        out_specs=(P("rows", "bx", "by", None), P(("rows", "bx", "by"))),
        check_vma=False,
    )
```

```python
import numpy as np
import jax
import jax.numpy as jnp
from jax import lax
from jax.experimental import pallas as pl
from jax.experimental.pallas import tpu as pltpu
from jax.sharding import PartitionSpec as P


def padded_2(x, sides, width):
    for axis, dim in sides:
        count, length = (lax.axis_size(axis), x.shape[dim])
        up = [(i, (i + 1) % count) for i in range(count)]
        down = [(j, i) for i, j in up]
        last = lax.slice_in_dim(x, length - width, length, axis=dim)
        leading = lax.slice_in_dim(x, 0, width, axis=dim)
        before = lax.ppermute(last, axis, up)
        after = lax.ppermute(leading, axis, down)
        x = jnp.concatenate([before, x, after], axis=dim)
    return x


def offset_table():
    listed = []
    for shift_z in range(-2, 3):
        for shift_x in range(-2, 3):
            for shift_y in range(-2, 3):
                if max(abs(shift_z), abs(shift_x), abs(shift_y)) == 2:
                    listed.append((shift_z, shift_x, shift_y))
    return listed


def sum_rounds(axes):
    rounds = []
    for axis in axes:
        count = lax.axis_size(axis)
        stride = 1
        while stride < count:
            group = min(4, count // stride)
            span = stride * group
            shifts = []
            for k in range(1, group):
                pairs = []
                for i in range(count):
                    block, rest = divmod(i, span)
                    pairs.append((i, block * span + (rest + k * stride) % span))
                shifts.append(pairs)
            rounds.append((axis, shifts))
            stride = span
    return rounds


def sum_round(x, step):
    axis, shifts = step
    total = x
    for pairs in shifts:
        total = total + lax.ppermute(x, axis, pairs)
    return total


def far_kernel(tab_ref, pad_ref, mask_ref, rs_ref, cs_ref, base_ref, out_ref, acc_ref, ysh_ref):
    rows = acc_ref.shape[0]
    lanes = mask_ref.shape[1]
    levels = 2
    chunk = levels * 8 * ysh_ref.shape[3]
    acc_ref[...] = jnp.zeros(acc_ref.shape, jnp.float32)
    for c in range(ysh_ref.shape[0]):
        for z in range(ysh_ref.shape[1]):
            ysh_ref[c, z] = pad_ref[z, :, c : c + ysh_ref.shape[3], :]
    lane = lax.broadcasted_iota(jnp.int32, (chunk, lanes), 1)

    def body(o, carry):
        a = tab_ref[3 * o]
        b = tab_ref[3 * o + 1]
        c = tab_ref[3 * o + 2]
        row_scale = rs_ref[pl.ds(o, 1), :]
        col_scale = cs_ref[pl.ds(o, 1), :]
        for q in range(rows // chunk):
            win = ysh_ref[c, pl.ds(a + levels * q, levels), pl.ds(b, 8), :, :].reshape(chunk, -1)
            gate = jnp.sum(
                jnp.where(lane == o, mask_ref[q * chunk : (q + 1) * chunk, :], 0.0), axis=1, keepdims=True
            )
            scaled = (win * gate * row_scale).astype(jnp.bfloat16)
            product = jnp.dot(scaled, base_ref[...], preferred_element_type=jnp.float32)
            acc_ref[q * chunk : (q + 1) * chunk, :] += product * col_scale
        return carry

    lax.fori_loop(0, tab_ref.shape[0] // 3, body, 0, unroll=7)
    out_ref[...] = acc_ref[...]


def far_field(padded, masks, row_scale, col_scale, base):
    rows = masks.shape[0]
    components = base.shape[1]
    table = np.array([[a + 2, b + 2, c + 2] for a, b, c in offset_table()], np.int32).reshape(-1)
    vmem = pltpu.MemorySpace.VMEM if hasattr(pltpu, "MemorySpace") else pltpu.VMEM
    smem = pltpu.MemorySpace.SMEM if hasattr(pltpu, "MemorySpace") else pltpu.SMEM
    return pl.pallas_call(
        far_kernel,
        out_shape=jax.ShapeDtypeStruct((rows, components), jnp.float32),
        in_specs=[pl.BlockSpec(memory_space=smem)] + [pl.BlockSpec(memory_space=vmem)] * 5,
        out_specs=pl.BlockSpec(memory_space=vmem),
        scratch_shapes=[
            pltpu.VMEM((rows, components), jnp.float32),
            pltpu.VMEM((5, padded.shape[0], padded.shape[1], padded.shape[2] - 4, components), jnp.float32),
        ],
        compiler_params=pltpu.CompilerParams(vmem_limit_bytes=48 * 1024 * 1024),
    )(jnp.asarray(table), padded, masks, row_scale, col_scale, base)


def device_body(
    pair_mult, pair_dens, pair_live, pair_box, inter_mask, row_scale, col_scale, base, lattice
):
    components = pair_mult.shape[1]
    depth, width_x, width_y, offsets = inter_mask.shape
    near_boxes = (depth + 4) * width_x * width_y
    weighted = (
        (pair_dens * pair_live.astype(jnp.float32))[:, None] * pair_mult.astype(jnp.float32)
    ).astype(jnp.bfloat16)
    cell_part = jnp.sum(weighted.astype(jnp.float32), 0)
    rounds = sum_rounds(("by", "bx", "rows"))
    cell = sum_round(sum_round(cell_part, rounds[0]), rounds[1])
    labels = lax.iota(jnp.int32, near_boxes)
    selector = (labels[:, None] == pair_box[None, :]).astype(jnp.bfloat16)
    partial_near = jnp.dot(selector, weighted, preferred_element_type=jnp.float32)
    partial_near = partial_near.reshape(depth + 4, width_x, width_y, components)
    count = lax.axis_size("rows")
    up = [(i, (i + 1) % count) for i in range(count)]
    down = [(j, i) for i, j in up]
    from_below = lax.ppermute(partial_near[depth:], "rows", up)
    from_above = lax.ppermute(partial_near[:4], "rows", down)
    zpad = partial_near.at[:4].add(from_below).at[depth:].add(from_above)
    padded = padded_2(zpad, (("bx", 1), ("by", 2)), 2)
    masks = inter_mask.reshape(depth * width_x * width_y, offsets).astype(jnp.float32)
    cell = sum_round(cell, rounds[2])
    far = far_field(padded, masks, row_scale, col_scale, base)
    cell, far, late_mult = lax.optimization_barrier((cell, far, pair_mult))
    near_far = padded_2(far.reshape(depth, width_x, width_y, components), (("rows", 0),), 2)
    cell = sum_round(cell, rounds[3])
    lattice_term = jnp.dot(cell, lattice, precision=lax.Precision.HIGHEST)
    near_locals = (near_far + lattice_term).astype(jnp.bfloat16)
    box_locals = near_locals[2 : 2 + depth]
    flat_locals = near_locals.reshape(near_boxes, components)
    onehot = (pair_box[:, None] == labels[None, :]).astype(jnp.bfloat16)
    picked_rows = jnp.dot(onehot, flat_locals, preferred_element_type=jnp.float32)
    pair_j = jnp.sum(late_mult.astype(jnp.float32) * picked_rows, -1)
    return (box_locals, pair_j)


def solution(mesh):
    return jax.shard_map(
        device_body,
        mesh=mesh,
        in_specs=(
            P(("rows", "bx", "by"), None),
            P(("rows", "bx", "by")),
            P(("rows", "bx", "by")),
            P(("rows", "bx", "by")),
            P("rows", "bx", "by", None),
            P(),
            P(),
            P(),
            P(),
        ),
        out_specs=(P("rows", "bx", "by", None), P(("rows", "bx", "by"))),
        check_vma=False,
    )
```

```python
import numpy as np
import jax
import jax.numpy as jnp
from jax import lax
from jax.experimental import pallas as pl
from jax.experimental.pallas import tpu as pltpu
from jax.sharding import PartitionSpec as P


def padded_2(x, sides, width):
    for axis, dim in sides:
        count, length = (lax.axis_size(axis), x.shape[dim])
        up = [(i, (i + 1) % count) for i in range(count)]
        down = [(j, i) for i, j in up]
        last = lax.slice_in_dim(x, length - width, length, axis=dim)
        leading = lax.slice_in_dim(x, 0, width, axis=dim)
        before = lax.ppermute(last, axis, up)
        after = lax.ppermute(leading, axis, down)
        x = jnp.concatenate([before, x, after], axis=dim)
    return x


def offset_table():
    listed = []
    for shift_z in range(-2, 3):
        for shift_x in range(-2, 3):
            for shift_y in range(-2, 3):
                if max(abs(shift_z), abs(shift_x), abs(shift_y)) == 2:
                    listed.append((shift_z, shift_x, shift_y))
    return listed


def sum_rounds(axes):
    rounds = []
    for axis in axes:
        count = lax.axis_size(axis)
        stride = 1
        while stride < count:
            group = min(4, count // stride)
            span = stride * group
            shifts = []
            for k in range(1, group):
                pairs = []
                for i in range(count):
                    block, rest = divmod(i, span)
                    pairs.append((i, block * span + (rest + k * stride) % span))
                shifts.append(pairs)
            rounds.append((axis, shifts))
            stride = span
    return rounds


def sum_round(x, step):
    axis, shifts = step
    total = x
    for pairs in shifts:
        total = total + lax.ppermute(x, axis, pairs)
    return total


def far_kernel(tab_ref, pad_ref, mask_ref, rs_ref, cs_ref, base_ref, out_ref, acc_ref, ysh_ref):
    rows = acc_ref.shape[0]
    lanes = mask_ref.shape[1]
    levels = 8
    chunk = levels * 8 * ysh_ref.shape[3]
    acc_ref[...] = jnp.zeros(acc_ref.shape, jnp.float32)
    for c in range(ysh_ref.shape[0]):
        for z in range(ysh_ref.shape[1]):
            ysh_ref[c, z] = pad_ref[z, :, c : c + ysh_ref.shape[3], :]
    lane = lax.broadcasted_iota(jnp.int32, (chunk, lanes), 1)

    def body(o, carry):
        a = tab_ref[3 * o]
        b = tab_ref[3 * o + 1]
        c = tab_ref[3 * o + 2]
        row_scale = rs_ref[pl.ds(o, 1), :]
        col_scale = cs_ref[pl.ds(o, 1), :]
        for q in range(rows // chunk):
            win = ysh_ref[c, pl.ds(a + levels * q, levels), pl.ds(b, 8), :, :].reshape(chunk, -1)
            gate = jnp.sum(
                jnp.where(lane == o, mask_ref[q * chunk : (q + 1) * chunk, :], 0.0), axis=1, keepdims=True
            )
            scaled = (win * gate * row_scale).astype(jnp.bfloat16)
            product = jnp.dot(scaled, base_ref[...], preferred_element_type=jnp.float32)
            acc_ref[q * chunk : (q + 1) * chunk, :] += product * col_scale
        return carry

    lax.fori_loop(0, tab_ref.shape[0] // 3, body, 0, unroll=14)
    out_ref[...] = acc_ref[...]


def far_field(padded, masks, row_scale, col_scale, base):
    rows = masks.shape[0]
    components = base.shape[1]
    table = np.array([[a + 2, b + 2, c + 2] for a, b, c in offset_table()], np.int32).reshape(-1)
    vmem = pltpu.MemorySpace.VMEM if hasattr(pltpu, "MemorySpace") else pltpu.VMEM
    smem = pltpu.MemorySpace.SMEM if hasattr(pltpu, "MemorySpace") else pltpu.SMEM
    return pl.pallas_call(
        far_kernel,
        out_shape=jax.ShapeDtypeStruct((rows, components), jnp.float32),
        in_specs=[pl.BlockSpec(memory_space=smem)] + [pl.BlockSpec(memory_space=vmem)] * 5,
        out_specs=pl.BlockSpec(memory_space=vmem),
        scratch_shapes=[
            pltpu.VMEM((rows, components), jnp.float32),
            pltpu.VMEM((5, padded.shape[0], padded.shape[1], padded.shape[2] - 4, components), jnp.float32),
        ],
        compiler_params=pltpu.CompilerParams(vmem_limit_bytes=48 * 1024 * 1024),
    )(jnp.asarray(table), padded, masks, row_scale, col_scale, base)


def device_body(
    pair_mult, pair_dens, pair_live, pair_box, inter_mask, row_scale, col_scale, base, lattice
):
    components = pair_mult.shape[1]
    depth, width_x, width_y, offsets = inter_mask.shape
    near_boxes = (depth + 4) * width_x * width_y
    weighted = (
        (pair_dens * pair_live.astype(jnp.float32))[:, None] * pair_mult.astype(jnp.float32)
    ).astype(jnp.bfloat16)
    cell_part = jnp.sum(weighted.astype(jnp.float32), 0)
    rounds = sum_rounds(("by", "bx", "rows"))
    cell = sum_round(sum_round(cell_part, rounds[0]), rounds[1])
    labels = lax.iota(jnp.int32, near_boxes)
    selector = (labels[:, None] == pair_box[None, :]).astype(jnp.bfloat16)
    partial_near = jnp.dot(selector, weighted, preferred_element_type=jnp.float32)
    partial_near = partial_near.reshape(depth + 4, width_x, width_y, components)
    count = lax.axis_size("rows")
    up = [(i, (i + 1) % count) for i in range(count)]
    down = [(j, i) for i, j in up]
    from_below = lax.ppermute(partial_near[depth:], "rows", up)
    from_above = lax.ppermute(partial_near[:4], "rows", down)
    zpad = partial_near.at[:4].add(from_below).at[depth:].add(from_above)
    padded = padded_2(zpad, (("bx", 1), ("by", 2)), 2)
    masks = inter_mask.reshape(depth * width_x * width_y, offsets).astype(jnp.float32)
    cell = sum_round(cell, rounds[2])
    far = far_field(padded, masks, row_scale, col_scale, base)
    cell, far = lax.optimization_barrier((cell, far))
    near_far = padded_2(far.reshape(depth, width_x, width_y, components), (("rows", 0),), 2)
    cell = sum_round(cell, rounds[3])
    lattice_term = jnp.dot(cell, lattice, precision=lax.Precision.HIGHEST)
    near_locals = (near_far + lattice_term).astype(jnp.bfloat16)
    box_locals = near_locals[2 : 2 + depth]
    flat_locals = near_locals.reshape(near_boxes, components)
    onehot = (pair_box[:, None] == labels[None, :]).astype(jnp.bfloat16)
    picked_rows = jnp.dot(onehot, flat_locals, preferred_element_type=jnp.float32)
    pair_j = jnp.sum(pair_mult.astype(jnp.float32) * picked_rows, -1)
    return (box_locals, pair_j)


def solution(mesh):
    return jax.shard_map(
        device_body,
        mesh=mesh,
        in_specs=(
            P(("rows", "bx", "by"), None),
            P(("rows", "bx", "by")),
            P(("rows", "bx", "by")),
            P(("rows", "bx", "by")),
            P("rows", "bx", "by", None),
            P(),
            P(),
            P(),
            P(),
        ),
        out_specs=(P("rows", "bx", "by", None), P(("rows", "bx", "by"))),
        check_vma=False,
    )
```
